512 devices in a mesh: particle: 16 (over z), field: 32 (over y, x, core).
Axes of the slice: x: 4, y: 4, z: 16, core: 2. Of those that a mesh axis runs over, the one named last changes fastest.
Arguments:
- vorticity: bfloat16 [16, 1024, 1024], P('particle', 'field'), may hold values from -6 to 6
- ancestors: int32 [16], replicated, may hold values from 0 to 15
- noise: bfloat16 [16, 1024, 1024], P('particle', 'field'), may hold values from -6 to 6
Outputs:
- forecast: float32 [16, 1024, 1024], P('particle', 'field')
The draws below stay inside these ranges and needn't reach their ends.
All inputs are finite; a program needn't handle non-finite values.
Results may differ from the reference program's by a relative error of at most 0.0003.
Values may be sent and summed in bfloat16 or wider, within the bound.
No kernel may reach another device: no remote copies, remote signals or barrier semaphores. Data moves between devices by JAX's collectives and lax.ppermute only.
A program may use at most 64 MiB of HBM per device.

```python
import math
import jax
import jax.numpy as jnp
import numpy as np
from jax import lax

GRID = 1024
PARTICLES = 16


def set_ends(drawn, rng, low, largest):
    extent = drawn.shape
    spot = [jax.random.randint(jax.random.fold_in(rng, axis), (), 0, extent[axis]) for axis in range(len(extent))]
    drawn = drawn.at[tuple(spot)].set(low)
    longest = extent.index(max(extent))
    spot[longest] = (spot[longest] + 1) % extent[longest]
    return drawn.at[tuple(spot)].set(largest)


def block_scale(own_key, extent, shards, least, largest):
    factor_of, own = 1.0, jax.random.fold_in(own_key, 6)
    for dim, shards_of in shards:
        steps = jnp.exp(jax.random.uniform(jax.random.fold_in(own, dim), (shards_of,), jnp.float32, least / len(shards), largest / len(shards)))
        factor_of = factor_of * jnp.repeat(steps, extent[dim] // shards_of).reshape([-1 if axis == dim else 1 for axis in range(len(extent))])
    return factor_of


def rank_bounds(count, lean):
    loads = [(1 << 20) // math.isqrt(standing ** lean) + 1 for standing in range(1, count + 1)]
    spread = 1 + sum(loads) // (1 << 30)
    return np.cumsum(np.array([max(1, weight // spread) for weight in loads]))


def skewed_ids(own_key, shape, number_of, skew):
    listing = rank_bounds(number_of, skew)
    lot = jax.random.randint(jax.random.fold_in(own_key, 1), shape, 0, int(listing[number_of - 1]))
    grade = jnp.searchsorted(jnp.asarray(listing, jnp.int32), lot, side="right")
    return jax.random.permutation(jax.random.fold_in(own_key, 2), number_of)[grade].astype(jnp.int32)


def normal_values(own_key, dims, deviation, most, shards=(), kind=jnp.bfloat16):
    array = deviation * jax.random.normal(own_key, dims, jnp.float32)
    if shards:
        array = array * block_scale(own_key, dims, shards, -0.22, 0.18)
    return jnp.clip(array, -most, most).astype(kind)


def setup_inputs(seed: int = 0) -> dict:
    streams_of = jax.random.split(jax.random.key(seed), 4)
    vorticity = normal_values(streams_of[0], (PARTICLES, GRID, GRID), 1.0, 6.0, ((0, 16), (1, 32)))
    ancestors = set_ends(skewed_ids(streams_of[1], (PARTICLES,), PARTICLES, 2), jax.random.fold_in(streams_of[1], 3), 0, PARTICLES - 1).astype(jnp.int32)
    noise = normal_values(streams_of[2], (PARTICLES, GRID, GRID), 1.0, 6.0, ((0, 16), (1, 32)))
    return dict(vorticity=vorticity, ancestors=ancestors, noise=noise)


PARENT_WEIGHT = 0.8
NOISE_WEIGHT = 0.6
VISCOSITY = 0.05
TIME_STEP = 0.1


def wave_tables(modes, length):
    signed = jnp.where(modes >= length // 2, modes - length, modes)
    wavenumber = (2.0 * math.pi / length) * signed.astype(jnp.float32)
    slope = jnp.where(modes == length // 2, jnp.zeros_like(wavenumber), wavenumber)
    retained = jnp.where(3 * jnp.abs(signed) < length, 1.0, 0.0).astype(jnp.float32)
    return wavenumber, slope, retained


def reference(vorticity, ancestors, noise):
    length = vorticity.shape[-1]
    wavenumber, slope, retained = wave_tables(jnp.arange(length, dtype=jnp.int32), length)
    squared = wavenumber[:, None] ** 2 + wavenumber[None, :] ** 2
    inverse_sq = jnp.where(squared > 0, 1.0 / jnp.where(squared > 0, squared, 1.0), 0.0)
    dealias = retained[:, None] * retained[None, :]
    spectrum_weight = 1.0 / (1.0 + squared)
    slope_x = slope[None, :]
    slope_y = slope[:, None]

    def tendency(spectral):
        potential = spectral * inverse_sq
        speed_x = jnp.fft.ifft2(1j * slope_y * potential).real
        speed_y = jnp.fft.ifft2(-1j * slope_x * potential).real
        grad_x = jnp.fft.ifft2(1j * slope_x * spectral).real
        grad_y = jnp.fft.ifft2(1j * slope_y * spectral).real
        advection = speed_x * grad_x + speed_y * grad_y
        return -dealias * jnp.fft.fft2(advection) - VISCOSITY * squared * spectral

    def propose_one(item):
        parent_index, particle_noise = item
        parent = jnp.take(vorticity, parent_index, axis=0).astype(jnp.float32)
        proposal = PARENT_WEIGHT * jnp.fft.fft2(parent) + NOISE_WEIGHT * spectrum_weight * jnp.fft.fft2(particle_noise.astype(jnp.float32))
        first_rate = tendency(proposal)
        midpoint = proposal + TIME_STEP * first_rate
        final = proposal + (0.5 * TIME_STEP) * (first_rate + tendency(midpoint))
        return jnp.fft.ifft2(final).real.astype(jnp.float32)

    return lax.map(propose_one, (ancestors, noise))
```

```python
import math

import jax
import jax.numpy as jnp
from jax import lax
from jax.sharding import PartitionSpec as P

PARENT_WEIGHT = 0.8
NOISE_WEIGHT = 0.6
VISCOSITY = 0.05
TIME_STEP = 0.1
HIGHEST = lax.Precision.HIGHEST


def turn_cos(turns, length):
    reduced = turns % length
    reduced = jnp.where(reduced >= length // 2, reduced - length, reduced)
    return jnp.cos((2.0 * math.pi / length) * reduced.astype(jnp.float32))


def slot_modes(length, parts):
    half = length // (2 * parts)
    order = lax.optimization_barrier(jnp.arange(length, dtype=jnp.int32))
    dest = order // (2 * half)
    t = order % (2 * half)
    mode = half * dest + t % half
    nyquist = order == half
    mode = jnp.where(nyquist, length // 2, mode)
    use_cos = (t < half) | nyquist
    return mode, use_cos


def row_tables(length, parts):
    mode, use_cos = slot_modes(length, parts)
    x = lax.optimization_barrier(jnp.arange(length, dtype=jnp.int32))
    shift = jnp.where(use_cos, 0, length // 4)
    turns_fwd = x[:, None] * mode[None, :] + shift[None, :]
    forward = turn_cos(turns_fwd, length)
    weight = jnp.where((mode == 0) | (mode == length // 2), 1.0, 2.0) / float(length * length)
    turns_inv = mode[:, None] * x[None, :] + shift[:, None]
    inverse = weight[:, None] * turn_cos(turns_inv, length)
    return forward, inverse


def column_table(length):
    n = lax.optimization_barrier(jnp.arange(length, dtype=jnp.int32))
    prod = n[:, None] * n[None, :]
    cosine = turn_cos(prod, length)
    sine = turn_cos(prod - length // 4, length)
    return jnp.concatenate([cosine, sine], axis=1)


def wave_tables(modes, length):
    signed = jnp.where(modes >= length // 2, modes - length, modes)
    wavenumber = 2.0 * math.pi / length * signed.astype(jnp.float32)
    slope = jnp.where(modes == length // 2, jnp.zeros_like(wavenumber), wavenumber)
    retained = jnp.where(3 * jnp.abs(signed) < length, 1.0, 0.0).astype(jnp.float32)
    return (wavenumber, slope, retained)


def local(vorticity, ancestors, noise):
    particle_count, row_count, length = vorticity.shape
    parts = lax.axis_size("field")
    half = length // (2 * parts)
    me = lax.axis_index("field")
    first_particle = lax.axis_index("particle") * particle_count

    row_fwd, row_inv = row_tables(length, parts)
    col_cs = column_table(length)

    slot = jnp.arange(half + 1, dtype=jnp.int32)
    mode_x = jnp.where(slot < half, half * me + slot, length // 2)
    mode_y = jnp.arange(length, dtype=jnp.int32)
    wave_x, slope_x, kept_x = wave_tables(mode_x, length)
    wave_y, slope_y, kept_y = wave_tables(mode_y, length)
    squared = wave_x[:, None] ** 2 + wave_y[None, :] ** 2
    inverse_sq = jnp.where(squared > 0, 1.0 / jnp.where(squared > 0, squared, 1.0), 0.0)
    dealias = kept_x[:, None] * kept_y[None, :]
    spectrum_weight = 1.0 / (1.0 + squared)
    slope_x = slope_x[:, None]
    slope_y = slope_y[None, :]
    on_first = me == 0
    pair_mask = jnp.where(on_first & (slot[:half] == 0), 0.0, 1.0)[:, None]
    nyquist_gate = jnp.where(on_first, 1.0, 0.0)

    def forward(fields):
        batch = fields.shape[0]
        rows = jnp.einsum("byx,xo->byo", fields, row_fwd, precision=HIGHEST)
        rows = rows.reshape(batch, row_count, parts, 2 * half)
        cols = lax.all_to_all(rows, "field", split_axis=2, concat_axis=1, tiled=True)
        cols = cols.reshape(batch, length, 2 * half)
        prod = jnp.einsum("byt,yk->btk", cols, col_cs, precision=HIGHEST)
        pc = prod[:, :, :length]
        ps = prod[:, :, length:]
        real = pc[:, :half] + pair_mask * ps[:, half:]
        imag = pair_mask * pc[:, half:] - ps[:, :half]
        ny_real = nyquist_gate * pc[:, half : half + 1]
        ny_imag = -nyquist_gate * ps[:, half : half + 1]
        real = jnp.concatenate([real, ny_real], axis=1)
        imag = jnp.concatenate([imag, ny_imag], axis=1)
        return real, imag

    def inverse(real, imag):
        batch = real.shape[0]
        stacked = jnp.concatenate([real, imag], axis=1)
        prod = jnp.einsum("bjm,mk->bjk", stacked, col_cs, precision=HIGHEST)
        n_slot = half + 1
        wr_c = prod[:, :n_slot, :length]
        wr_s = prod[:, :n_slot, length:]
        wi_c = prod[:, n_slot:, :length]
        wi_s = prod[:, n_slot:, length:]
        z_real = wr_c - wi_s
        z_imag = wr_s + wi_c
        first_imag = jnp.where(on_first, z_real[:, half : half + 1], z_imag[:, 0:1])
        send = jnp.concatenate([z_real[:, :half], first_imag, z_imag[:, 1:half]], axis=1)
        send = send.reshape(batch, 2 * half, parts, row_count)
        back = lax.all_to_all(send, "field", split_axis=2, concat_axis=1, tiled=True)
        back = back.reshape(batch, length, row_count)
        return jnp.einsum("bsy,sx->byx", back, row_inv, precision=HIGHEST)

    def tendency(real, imag):
        pot_r = real * inverse_sq
        pot_i = imag * inverse_sq
        fr = jnp.stack(
            [
                -slope_y * pot_i,
                slope_x * pot_i,
                -slope_x * imag,
                -slope_y * imag,
            ],
            axis=0,
        )
        fi = jnp.stack(
            [
                slope_y * pot_r,
                -slope_x * pot_r,
                slope_x * real,
                slope_y * real,
            ],
            axis=0,
        )
        physical = inverse(fr, fi)
        advection = physical[0:1] * physical[2:3] + physical[1:2] * physical[3:4]
        ar, ai = forward(advection)
        return (
            -dealias * ar[0] - VISCOSITY * squared * real,
            -dealias * ai[0] - VISCOSITY * squared * imag,
        )

    noise_r, noise_i = forward(noise.astype(jnp.float32))
    shard_rows = lax.all_gather(vorticity, "particle", axis=0, tiled=True)
    wanted = lax.dynamic_slice_in_dim(ancestors, first_particle, particle_count)
    parents = jnp.take(shard_rows, wanted, axis=0).astype(jnp.float32)
    par_r, par_i = forward(parents)

    prop_r = PARENT_WEIGHT * par_r[0] + NOISE_WEIGHT * spectrum_weight * noise_r[0]
    prop_i = PARENT_WEIGHT * par_i[0] + NOISE_WEIGHT * spectrum_weight * noise_i[0]
    rate1_r, rate1_i = tendency(prop_r, prop_i)
    mid_r = prop_r + TIME_STEP * rate1_r
    mid_i = prop_i + TIME_STEP * rate1_i
    rate2_r, rate2_i = tendency(mid_r, mid_i)
    fin_r = prop_r + 0.5 * TIME_STEP * (rate1_r + rate2_r)
    fin_i = prop_i + 0.5 * TIME_STEP * (rate1_i + rate2_i)
    return inverse(fin_r[None], fin_i[None])


def solution(mesh):
    placed = (P("particle", "field", None), P(), P("particle", "field", None))
    return jax.shard_map(
        local, mesh=mesh, in_specs=placed, out_specs=P("particle", "field", None), check_vma=False
    )
```

```python
import math

import jax
import jax.numpy as jnp
from jax import lax
from jax.sharding import PartitionSpec as P

PARENT_WEIGHT = 0.8
NOISE_WEIGHT = 0.6
VISCOSITY = 0.05
TIME_STEP = 0.1
HIGHEST = lax.Precision.HIGHEST


def turn_phase(turns, length):
    reduced = turns % length
    reduced = jnp.where(reduced >= length // 2, reduced - length, reduced)
    angle = (2.0 * math.pi / length) * reduced.astype(jnp.float32)
    return jnp.cos(angle), jnp.sin(angle)


def split_cos(coarse, fine):
    return coarse[0] * fine[0] - coarse[1] * fine[1]


def split_sin(coarse, fine):
    return coarse[1] * fine[0] + coarse[0] * fine[1]


def slot_modes(length, parts):
    half = length // (2 * parts)
    order = lax.optimization_barrier(jnp.arange(length, dtype=jnp.int32))
    dest = order // (2 * half)
    t = order % (2 * half)
    mode = half * dest + t % half
    nyquist = order == half
    mode = jnp.where(nyquist, length // 2, mode)
    use_cos = (t < half) | nyquist
    return mode, use_cos


def grid_split(length):
    fine = 1 << ((length.bit_length() - 1) // 2)
    return fine, length // fine


def row_tables(length, parts):
    mode, use_cos = slot_modes(length, parts)
    fine, coarse = grid_split(length)
    hi = lax.optimization_barrier(jnp.arange(coarse, dtype=jnp.int32)) * fine
    lo = lax.optimization_barrier(jnp.arange(fine, dtype=jnp.int32))
    shift = jnp.where(use_cos, 0, length // 4)
    big = turn_phase(hi[:, None] * mode[None, :], length)
    small = turn_phase(lo[:, None] * mode[None, :] + shift[None, :], length)
    forward = split_cos(
        (big[0][:, None, :], big[1][:, None, :]), (small[0][None], small[1][None])
    ).reshape(length, length)
    weight = jnp.where((mode == 0) | (mode == length // 2), 1.0, 2.0) / float(length * length)
    big = turn_phase(mode[:, None] * hi[None, :], length)
    small = turn_phase(mode[:, None] * lo[None, :] + shift[:, None], length)
    inverse = split_cos(
        (big[0][:, :, None], big[1][:, :, None]), (small[0][:, None, :], small[1][:, None, :])
    ).reshape(length, length)
    inverse = weight[:, None] * inverse
    return lax.optimization_barrier((forward, inverse))


def column_table(length):
    fine, coarse = grid_split(length)
    hi = lax.optimization_barrier(jnp.arange(coarse, dtype=jnp.int32)) * fine
    lo = lax.optimization_barrier(jnp.arange(fine, dtype=jnp.int32))
    n = lax.optimization_barrier(jnp.arange(length, dtype=jnp.int32))
    big = turn_phase(hi[:, None] * n[None, :], length)
    small = turn_phase(lo[:, None] * n[None, :], length)
    big = (big[0][:, None, :], big[1][:, None, :])
    small = (small[0][None], small[1][None])
    cosine = split_cos(big, small).reshape(length, length)
    sine = split_sin(big, small).reshape(length, length)
    return lax.optimization_barrier(jnp.concatenate([cosine, sine], axis=1))


def wave_tables(modes, length):
    signed = jnp.where(modes >= length // 2, modes - length, modes)
    wavenumber = 2.0 * math.pi / length * signed.astype(jnp.float32)
    slope = jnp.where(modes == length // 2, jnp.zeros_like(wavenumber), wavenumber)
    retained = jnp.where(3 * jnp.abs(signed) < length, 1.0, 0.0).astype(jnp.float32)
    return (wavenumber, slope, retained)


def local(vorticity, ancestors, noise):
    particle_count, row_count, length = vorticity.shape
    parts = lax.axis_size("field")
    half = length // (2 * parts)
    me = lax.axis_index("field")
    first_particle = lax.axis_index("particle") * particle_count

    row_fwd, row_inv = row_tables(length, parts)
    col_cs = column_table(length)

    slot = jnp.arange(half + 1, dtype=jnp.int32)
    mode_x = jnp.where(slot < half, half * me + slot, length // 2)
    mode_y = jnp.arange(length, dtype=jnp.int32)
    wave_x, slope_x, kept_x = wave_tables(mode_x, length)
    wave_y, slope_y, kept_y = wave_tables(mode_y, length)
    squared = wave_x[:, None] ** 2 + wave_y[None, :] ** 2
    inverse_sq = jnp.where(squared > 0, 1.0 / jnp.where(squared > 0, squared, 1.0), 0.0)
    dealias = kept_x[:, None] * kept_y[None, :]
    spectrum_weight = 1.0 / (1.0 + squared)
    slope_x = slope_x[:, None]
    slope_y = slope_y[None, :]
    on_first = me == 0
    pair_mask = jnp.where(on_first & (slot[:half] == 0), 0.0, 1.0)[:, None]
    nyquist_gate = jnp.where(on_first, 1.0, 0.0)

    def forward(fields):
        batch = fields.shape[0]
        rows = jnp.einsum("byx,xo->byo", fields, row_fwd, precision=HIGHEST)
        rows = rows.reshape(batch, row_count, parts, 2 * half)
        cols = lax.all_to_all(rows, "field", split_axis=2, concat_axis=1, tiled=True)
        cols = cols.reshape(batch, length, 2 * half)
        prod = jnp.einsum("byt,yk->btk", cols, col_cs, precision=HIGHEST)
        pc = prod[:, :, :length]
        ps = prod[:, :, length:]
        real = pc[:, :half] + pair_mask * ps[:, half:]
        imag = pair_mask * pc[:, half:] - ps[:, :half]
        ny_real = nyquist_gate * pc[:, half : half + 1]
        ny_imag = -nyquist_gate * ps[:, half : half + 1]
        real = jnp.concatenate([real, ny_real], axis=1)
        imag = jnp.concatenate([imag, ny_imag], axis=1)
        return real, imag

    def inverse(real, imag):
        batch = real.shape[0]
        stacked = jnp.concatenate([real, imag], axis=1)
        prod = jnp.einsum("bjm,mk->bjk", stacked, col_cs, precision=HIGHEST)
        n_slot = half + 1
        wr_c = prod[:, :n_slot, :length]
        wr_s = prod[:, :n_slot, length:]
        wi_c = prod[:, n_slot:, :length]
        wi_s = prod[:, n_slot:, length:]
        z_real = wr_c - wi_s
        z_imag = wr_s + wi_c
        first_imag = jnp.where(on_first, z_real[:, half : half + 1], z_imag[:, 0:1])
        send = jnp.concatenate([z_real[:, :half], first_imag, z_imag[:, 1:half]], axis=1)
        send = send.reshape(batch, 2 * half, parts, row_count)
        back = lax.all_to_all(send, "field", split_axis=2, concat_axis=1, tiled=True)
        back = back.reshape(batch, length, row_count)
        return jnp.einsum("bsy,sx->byx", back, row_inv, precision=HIGHEST)

    def tendency(real, imag):
        pot_r = real * inverse_sq
        pot_i = imag * inverse_sq
        fr = jnp.stack(
            [
                -slope_y * pot_i,
                slope_x * pot_i,
                -slope_x * imag,
                -slope_y * imag,
            ],
            axis=0,
        )
        fi = jnp.stack(
            [
                slope_y * pot_r,
                -slope_x * pot_r,
                slope_x * real,
                slope_y * real,
            ],
            axis=0,
        )
        physical = inverse(fr, fi)
        advection = physical[0:1] * physical[2:3] + physical[1:2] * physical[3:4]
        ar, ai = forward(advection)
        return (
            -dealias * ar[0] - VISCOSITY * squared * real,
            -dealias * ai[0] - VISCOSITY * squared * imag,
        )

    noise_r, noise_i = forward(noise.astype(jnp.float32))
    shard_rows = lax.all_gather(vorticity, "particle", axis=0, tiled=True)
    wanted = lax.dynamic_slice_in_dim(ancestors, first_particle, particle_count)
    parents = jnp.take(shard_rows, wanted, axis=0).astype(jnp.float32)
    par_r, par_i = forward(parents)

    prop_r = PARENT_WEIGHT * par_r[0] + NOISE_WEIGHT * spectrum_weight * noise_r[0]
    prop_i = PARENT_WEIGHT * par_i[0] + NOISE_WEIGHT * spectrum_weight * noise_i[0]
    rate1_r, rate1_i = tendency(prop_r, prop_i)
    mid_r = prop_r + TIME_STEP * rate1_r
    mid_i = prop_i + TIME_STEP * rate1_i
    rate2_r, rate2_i = tendency(mid_r, mid_i)
    fin_r = prop_r + 0.5 * TIME_STEP * (rate1_r + rate2_r)
    fin_i = prop_i + 0.5 * TIME_STEP * (rate1_i + rate2_i)
    return inverse(fin_r[None], fin_i[None])


def solution(mesh):
    placed = (P("particle", "field", None), P(), P("particle", "field", None))
    return jax.shard_map(
        local, mesh=mesh, in_specs=placed, out_specs=P("particle", "field", None), check_vma=False
    )
```

```python
import math

import jax
import jax.numpy as jnp
from jax import lax
from jax.sharding import PartitionSpec as P

PARENT_WEIGHT = 0.8
NOISE_WEIGHT = 0.6
VISCOSITY = 0.05
TIME_STEP = 0.1
HIGHEST = lax.Precision.HIGH


def turn_phase(turns, length):
    reduced = turns % length
    reduced = jnp.where(reduced >= length // 2, reduced - length, reduced)
    angle = (2.0 * math.pi / length) * reduced.astype(jnp.float32)
    return jnp.cos(angle), jnp.sin(angle)


def split_cos(coarse, fine):
    return coarse[0] * fine[0] - coarse[1] * fine[1]


def split_sin(coarse, fine):
    return coarse[1] * fine[0] + coarse[0] * fine[1]


def slot_modes(length, parts):
    half = length // (2 * parts)
    order = lax.optimization_barrier(jnp.arange(length, dtype=jnp.int32))
    dest = order // (2 * half)
    t = order % (2 * half)
    mode = half * dest + t % half
    nyquist = order == half
    mode = jnp.where(nyquist, length // 2, mode)
    use_cos = (t < half) | nyquist
    return mode, use_cos


def grid_split(length):
    fine = 1 << ((length.bit_length() - 1) // 2)
    return fine, length // fine


def row_tables(length, parts):
    mode, use_cos = slot_modes(length, parts)
    fine, coarse = grid_split(length)
    hi = lax.optimization_barrier(jnp.arange(coarse, dtype=jnp.int32)) * fine
    lo = lax.optimization_barrier(jnp.arange(fine, dtype=jnp.int32))
    shift = jnp.where(use_cos, 0, length // 4)
    big = turn_phase(hi[:, None] * mode[None, :], length)
    small = turn_phase(lo[:, None] * mode[None, :] + shift[None, :], length)
    forward = split_cos(
        (big[0][:, None, :], big[1][:, None, :]), (small[0][None], small[1][None])
    ).reshape(length, length)
    weight = jnp.where((mode == 0) | (mode == length // 2), 1.0, 2.0) / float(length * length)
    big = turn_phase(mode[:, None] * hi[None, :], length)
    small = turn_phase(mode[:, None] * lo[None, :] + shift[:, None], length)
    inverse = split_cos(
        (big[0][:, :, None], big[1][:, :, None]), (small[0][:, None, :], small[1][:, None, :])
    ).reshape(length, length)
    inverse = weight[:, None] * inverse
    return lax.optimization_barrier((forward, inverse))


def column_table(length):
    fine, coarse = grid_split(length)
    hi = lax.optimization_barrier(jnp.arange(coarse, dtype=jnp.int32)) * fine
    lo = lax.optimization_barrier(jnp.arange(fine, dtype=jnp.int32))
    n = lax.optimization_barrier(jnp.arange(length, dtype=jnp.int32))
    big = turn_phase(hi[:, None] * n[None, :], length)
    small = turn_phase(lo[:, None] * n[None, :], length)
    big = (big[0][:, None, :], big[1][:, None, :])
    small = (small[0][None], small[1][None])
    cosine = split_cos(big, small).reshape(length, length)
    sine = split_sin(big, small).reshape(length, length)
    return lax.optimization_barrier(jnp.concatenate([cosine, sine], axis=1))


def wave_tables(modes, length):
    signed = jnp.where(modes >= length // 2, modes - length, modes)
    wavenumber = 2.0 * math.pi / length * signed.astype(jnp.float32)
    slope = jnp.where(modes == length // 2, jnp.zeros_like(wavenumber), wavenumber)
    retained = jnp.where(3 * jnp.abs(signed) < length, 1.0, 0.0).astype(jnp.float32)
    return (wavenumber, slope, retained)


def local(vorticity, ancestors, noise):
    particle_count, row_count, length = vorticity.shape
    parts = lax.axis_size("field")
    half = length // (2 * parts)
    me = lax.axis_index("field")
    first_particle = lax.axis_index("particle") * particle_count

    row_fwd, row_inv = row_tables(length, parts)
    col_cs = column_table(length)

    slot = jnp.arange(half + 1, dtype=jnp.int32)
    mode_x = jnp.where(slot < half, half * me + slot, length // 2)
    mode_y = jnp.arange(length, dtype=jnp.int32)
    wave_x, slope_x, kept_x = wave_tables(mode_x, length)
    wave_y, slope_y, kept_y = wave_tables(mode_y, length)
    squared = wave_x[:, None] ** 2 + wave_y[None, :] ** 2
    inverse_sq = jnp.where(squared > 0, 1.0 / jnp.where(squared > 0, squared, 1.0), 0.0)
    dealias = kept_x[:, None] * kept_y[None, :]
    spectrum_weight = 1.0 / (1.0 + squared)
    slope_x = slope_x[:, None]
    slope_y = slope_y[None, :]
    on_first = me == 0
    pair_mask = jnp.where(on_first & (slot[:half] == 0), 0.0, 1.0)[:, None]
    nyquist_gate = jnp.where(on_first, 1.0, 0.0)

    def forward(fields):
        batch = fields.shape[0]
        rows = jnp.einsum("byx,xo->byo", fields, row_fwd, precision=HIGHEST)
        rows = rows.reshape(batch, row_count, parts, 2 * half)
        cols = lax.all_to_all(rows, "field", split_axis=2, concat_axis=1, tiled=True)
        cols = cols.reshape(batch, length, 2 * half)
        prod = jnp.einsum("byt,yk->btk", cols, col_cs, precision=HIGHEST)
        pc = prod[:, :, :length]
        ps = prod[:, :, length:]
        real = pc[:, :half] + pair_mask * ps[:, half:]
        imag = pair_mask * pc[:, half:] - ps[:, :half]
        ny_real = nyquist_gate * pc[:, half : half + 1]
        ny_imag = -nyquist_gate * ps[:, half : half + 1]
        real = jnp.concatenate([real, ny_real], axis=1)
        imag = jnp.concatenate([imag, ny_imag], axis=1)
        return real, imag

    def inverse(real, imag):
        batch = real.shape[0]
        stacked = jnp.concatenate([real, imag], axis=1)
        prod = jnp.einsum("bjm,mk->bjk", stacked, col_cs, precision=HIGHEST)
        n_slot = half + 1
        wr_c = prod[:, :n_slot, :length]
        wr_s = prod[:, :n_slot, length:]
        wi_c = prod[:, n_slot:, :length]
        wi_s = prod[:, n_slot:, length:]
        z_real = wr_c - wi_s
        z_imag = wr_s + wi_c
        first_imag = jnp.where(on_first, z_real[:, half : half + 1], z_imag[:, 0:1])
        send = jnp.concatenate([z_real[:, :half], first_imag, z_imag[:, 1:half]], axis=1)
        send = send.reshape(batch, 2 * half, parts, row_count)
        back = lax.all_to_all(send, "field", split_axis=2, concat_axis=1, tiled=True)
        back = back.reshape(batch, length, row_count)
        return jnp.einsum("bsy,sx->byx", back, row_inv, precision=HIGHEST)

    def tendency(real, imag):
        pot_r = real * inverse_sq
        pot_i = imag * inverse_sq
        fr = jnp.stack(
            [
                -slope_y * pot_i,
                slope_x * pot_i,
                -slope_x * imag,
                -slope_y * imag,
            ],
            axis=0,
        )
        fi = jnp.stack(
            [
                slope_y * pot_r,
                -slope_x * pot_r,
                slope_x * real,
                slope_y * real,
            ],
            axis=0,
        )
        physical = inverse(fr, fi)
        advection = physical[0:1] * physical[2:3] + physical[1:2] * physical[3:4]
        ar, ai = forward(advection)
        return (
            -dealias * ar[0] - VISCOSITY * squared * real,
            -dealias * ai[0] - VISCOSITY * squared * imag,
        )

    noise_r, noise_i = forward(noise.astype(jnp.float32))
    shard_rows = lax.all_gather(vorticity, "particle", axis=0, tiled=True)
    wanted = lax.dynamic_slice_in_dim(ancestors, first_particle, particle_count)
    parents = jnp.take(shard_rows, wanted, axis=0).astype(jnp.float32)
    par_r, par_i = forward(parents)

    prop_r = PARENT_WEIGHT * par_r[0] + NOISE_WEIGHT * spectrum_weight * noise_r[0]
    prop_i = PARENT_WEIGHT * par_i[0] + NOISE_WEIGHT * spectrum_weight * noise_i[0]
    rate1_r, rate1_i = tendency(prop_r, prop_i)
    mid_r = prop_r + TIME_STEP * rate1_r
    mid_i = prop_i + TIME_STEP * rate1_i
    rate2_r, rate2_i = tendency(mid_r, mid_i)
    fin_r = prop_r + 0.5 * TIME_STEP * (rate1_r + rate2_r)
    fin_i = prop_i + 0.5 * TIME_STEP * (rate1_i + rate2_i)
    return inverse(fin_r[None], fin_i[None])


def solution(mesh):
    placed = (P("particle", "field", None), P(), P("particle", "field", None))
    return jax.shard_map(
        local, mesh=mesh, in_specs=placed, out_specs=P("particle", "field", None), check_vma=False
    )
```

```python
import math

import jax
import jax.numpy as jnp
from jax import lax
from jax.sharding import PartitionSpec as P

PARENT_WEIGHT = 0.8
NOISE_WEIGHT = 0.6
VISCOSITY = 0.05
TIME_STEP = 0.1
HIGHEST = lax.Precision.HIGH


def turn_phase(turns, length):
    reduced = turns % length
    reduced = jnp.where(reduced >= length // 2, reduced - length, reduced)
    angle = (2.0 * math.pi / length) * reduced.astype(jnp.float32)
    return jnp.cos(angle), jnp.sin(angle)


def split_cos(coarse, fine):
    return coarse[0] * fine[0] - coarse[1] * fine[1]


def split_sin(coarse, fine):
    return coarse[1] * fine[0] + coarse[0] * fine[1]


def slot_modes(length, parts):
    half = length // (2 * parts)
    order = lax.optimization_barrier(jnp.arange(length, dtype=jnp.int32))
    dest = order // (2 * half)
    t = order % (2 * half)
    mode = half * dest + t % half
    nyquist = order == half
    mode = jnp.where(nyquist, length // 2, mode)
    use_cos = (t < half) | nyquist
    return mode, use_cos


def grid_split(length):
    fine = 1 << ((length.bit_length() - 1) // 2)
    return fine, length // fine


def row_tables(length, parts):
    mode, use_cos = slot_modes(length, parts)
    fine, coarse = grid_split(length)
    hi = lax.optimization_barrier(jnp.arange(coarse, dtype=jnp.int32)) * fine
    lo = lax.optimization_barrier(jnp.arange(fine, dtype=jnp.int32))
    shift = jnp.where(use_cos, 0, length // 4)
    big = turn_phase(hi[:, None] * mode[None, :], length)
    small = turn_phase(lo[:, None] * mode[None, :] + shift[None, :], length)
    forward = split_cos(
        (big[0][:, None, :], big[1][:, None, :]), (small[0][None], small[1][None])
    ).reshape(length, length)
    weight = jnp.where((mode == 0) | (mode == length // 2), 1.0, 2.0) / float(length * length)
    big = turn_phase(mode[:, None] * hi[None, :], length)
    small = turn_phase(mode[:, None] * lo[None, :] + shift[:, None], length)
    inverse = split_cos(
        (big[0][:, :, None], big[1][:, :, None]), (small[0][:, None, :], small[1][:, None, :])
    ).reshape(length, length)
    inverse = weight[:, None] * inverse
    return lax.optimization_barrier((forward, inverse))


def column_table(length):
    fine, coarse = grid_split(length)
    hi = lax.optimization_barrier(jnp.arange(coarse, dtype=jnp.int32)) * fine
    lo = lax.optimization_barrier(jnp.arange(fine, dtype=jnp.int32))
    n = lax.optimization_barrier(jnp.arange(length, dtype=jnp.int32))
    big = turn_phase(hi[:, None] * n[None, :], length)
    small = turn_phase(lo[:, None] * n[None, :], length)
    big = (big[0][:, None, :], big[1][:, None, :])
    small = (small[0][None], small[1][None])
    cosine = split_cos(big, small).reshape(length, length)
    sine = split_sin(big, small).reshape(length, length)
    return lax.optimization_barrier(jnp.concatenate([cosine, sine], axis=1))


def wave_tables(modes, length):
    signed = jnp.where(modes >= length // 2, modes - length, modes)
    wavenumber = 2.0 * math.pi / length * signed.astype(jnp.float32)
    slope = jnp.where(modes == length // 2, jnp.zeros_like(wavenumber), wavenumber)
    retained = jnp.where(3 * jnp.abs(signed) < length, 1.0, 0.0).astype(jnp.float32)
    return (wavenumber, slope, retained)


def fetch_parent(vorticity, ancestors, first_particle):
    count = lax.axis_size("particle")
    if vorticity.shape[0] != 1 or count & (count - 1):
        shard_rows = lax.all_gather(vorticity, "particle", axis=0, tiled=True)
        wanted = lax.dynamic_slice_in_dim(ancestors, first_particle, vorticity.shape[0])
        return jnp.take(shard_rows, wanted, axis=0)
    low = 1 << ((count.bit_length() - 1) // 2)
    high = count // low
    me = lax.axis_index("particle")
    my_high, my_low = me // low, me % low
    held = [vorticity]
    for step in range(1, high):
        perm = [(i, ((i // low + step) % high) * low + i % low) for i in range(count)]
        held.append(lax.ppermute(vorticity, "particle", perm))
    held = jnp.concatenate(held, axis=0)
    forwarded = []
    for step in range(1, low):
        target = my_high * low + (my_low + step) % low
        need = ancestors[target]
        pick = (my_high - need // low) % high
        chosen = lax.dynamic_index_in_dim(held, pick, axis=0, keepdims=True)
        perm = [(i, (i // low) * low + (i % low + step) % low) for i in range(count)]
        forwarded.append(lax.ppermute(chosen, "particle", perm))
    candidates = jnp.concatenate([held] + forwarded, axis=0)
    need = ancestors[me]
    need_high, need_low = need // low, need % low
    index = jnp.where(
        need_low == my_low,
        (my_high - need_high) % high,
        high + (my_low - need_low) % low - 1,
    )
    return lax.dynamic_index_in_dim(candidates, index, axis=0, keepdims=True)


def local(vorticity, ancestors, noise):
    particle_count, row_count, length = vorticity.shape
    parts = lax.axis_size("field")
    half = length // (2 * parts)
    me = lax.axis_index("field")
    first_particle = lax.axis_index("particle") * particle_count

    row_fwd, row_inv = row_tables(length, parts)
    col_cs = column_table(length)

    slot = jnp.arange(half + 1, dtype=jnp.int32)
    mode_x = jnp.where(slot < half, half * me + slot, length // 2)
    mode_y = jnp.arange(length, dtype=jnp.int32)
    wave_x, slope_x, kept_x = wave_tables(mode_x, length)
    wave_y, slope_y, kept_y = wave_tables(mode_y, length)
    squared = wave_x[:, None] ** 2 + wave_y[None, :] ** 2
    inverse_sq = jnp.where(squared > 0, 1.0 / jnp.where(squared > 0, squared, 1.0), 0.0)
    dealias = kept_x[:, None] * kept_y[None, :]
    spectrum_weight = 1.0 / (1.0 + squared)
    slope_x = slope_x[:, None]
    slope_y = slope_y[None, :]
    on_first = me == 0
    pair_mask = jnp.where(on_first & (slot[:half] == 0), 0.0, 1.0)[:, None]
    nyquist_gate = jnp.where(on_first, 1.0, 0.0)

    def forward(fields):
        batch = fields.shape[0]
        rows = jnp.einsum("byx,xo->byo", fields, row_fwd, precision=HIGHEST)
        rows = rows.reshape(batch, row_count, parts, 2 * half)
        cols = lax.all_to_all(rows, "field", split_axis=2, concat_axis=1, tiled=True)
        cols = cols.reshape(batch, length, 2 * half)
        prod = jnp.einsum("byt,yk->btk", cols, col_cs, precision=HIGHEST)
        pc = prod[:, :, :length]
        ps = prod[:, :, length:]
        real = pc[:, :half] + pair_mask * ps[:, half:]
        imag = pair_mask * pc[:, half:] - ps[:, :half]
        ny_real = nyquist_gate * pc[:, half : half + 1]
        ny_imag = -nyquist_gate * ps[:, half : half + 1]
        real = jnp.concatenate([real, ny_real], axis=1)
        imag = jnp.concatenate([imag, ny_imag], axis=1)
        return real, imag

    def inverse(real, imag):
        batch = real.shape[0]
        stacked = jnp.concatenate([real, imag], axis=1)
        prod = jnp.einsum("bjm,mk->bjk", stacked, col_cs, precision=HIGHEST)
        n_slot = half + 1
        wr_c = prod[:, :n_slot, :length]
        wr_s = prod[:, :n_slot, length:]
        wi_c = prod[:, n_slot:, :length]
        wi_s = prod[:, n_slot:, length:]
        z_real = wr_c - wi_s
        z_imag = wr_s + wi_c
        first_imag = jnp.where(on_first, z_real[:, half : half + 1], z_imag[:, 0:1])
        send = jnp.concatenate([z_real[:, :half], first_imag, z_imag[:, 1:half]], axis=1)
        send = send.reshape(batch, 2 * half, parts, row_count)
        back = lax.all_to_all(send, "field", split_axis=2, concat_axis=1, tiled=True)
        back = back.reshape(batch, length, row_count)
        return jnp.einsum("bsy,sx->byx", back, row_inv, precision=HIGHEST)

    def tendency(real, imag):
        pot_r = real * inverse_sq
        pot_i = imag * inverse_sq
        fr = jnp.stack(
            [
                -slope_y * pot_i,
                slope_x * pot_i,
                -slope_x * imag,
                -slope_y * imag,
            ],
            axis=0,
        )
        fi = jnp.stack(
            [
                slope_y * pot_r,
                -slope_x * pot_r,
                slope_x * real,
                slope_y * real,
            ],
            axis=0,
        )
        physical = inverse(fr, fi)
        advection = physical[0:1] * physical[2:3] + physical[1:2] * physical[3:4]
        ar, ai = forward(advection)
        return (
            -dealias * ar[0] - VISCOSITY * squared * real,
            -dealias * ai[0] - VISCOSITY * squared * imag,
        )

    noise_r, noise_i = forward(noise.astype(jnp.float32))
    parents = fetch_parent(vorticity, ancestors, first_particle).astype(jnp.float32)
    par_r, par_i = forward(parents)

    prop_r = PARENT_WEIGHT * par_r[0] + NOISE_WEIGHT * spectrum_weight * noise_r[0]
    prop_i = PARENT_WEIGHT * par_i[0] + NOISE_WEIGHT * spectrum_weight * noise_i[0]
    rate1_r, rate1_i = tendency(prop_r, prop_i)
    mid_r = prop_r + TIME_STEP * rate1_r
    mid_i = prop_i + TIME_STEP * rate1_i
    rate2_r, rate2_i = tendency(mid_r, mid_i)
    fin_r = prop_r + 0.5 * TIME_STEP * (rate1_r + rate2_r)
    fin_i = prop_i + 0.5 * TIME_STEP * (rate1_i + rate2_i)
    return inverse(fin_r[None], fin_i[None])


def solution(mesh):
    placed = (P("particle", "field", None), P(), P("particle", "field", None))
    return jax.shard_map(
        local, mesh=mesh, in_specs=placed, out_specs=P("particle", "field", None), check_vma=False
    )
```

```python
import math

import jax
import jax.numpy as jnp
from jax import lax
from jax.sharding import Mesh, PartitionSpec as P

PARENT_WEIGHT = 0.8
NOISE_WEIGHT = 0.6
VISCOSITY = 0.05
TIME_STEP = 0.1
HIGHEST = lax.Precision.HIGH


def turn_phase(turns, length):
    reduced = turns % length
    reduced = jnp.where(reduced >= length // 2, reduced - length, reduced)
    angle = (2.0 * math.pi / length) * reduced.astype(jnp.float32)
    return jnp.cos(angle), jnp.sin(angle)


def split_cos(coarse, fine):
    return coarse[0] * fine[0] - coarse[1] * fine[1]


def split_sin(coarse, fine):
    return coarse[1] * fine[0] + coarse[0] * fine[1]


def slot_modes(length, parts):
    half = length // (2 * parts)
    order = lax.optimization_barrier(jnp.arange(length, dtype=jnp.int32))
    dest = order // (2 * half)
    t = order % (2 * half)
    mode = half * dest + t % half
    nyquist = order == half
    mode = jnp.where(nyquist, length // 2, mode)
    use_cos = (t < half) | nyquist
    return mode, use_cos


def grid_split(length):
    fine = 1 << ((length.bit_length() - 1) // 2)
    return fine, length // fine


def row_tables(length, parts):
    mode, use_cos = slot_modes(length, parts)
    fine, coarse = grid_split(length)
    hi = lax.optimization_barrier(jnp.arange(coarse, dtype=jnp.int32)) * fine
    lo = lax.optimization_barrier(jnp.arange(fine, dtype=jnp.int32))
    shift = jnp.where(use_cos, 0, length // 4)
    big = turn_phase(hi[:, None] * mode[None, :], length)
    small = turn_phase(lo[:, None] * mode[None, :] + shift[None, :], length)
    forward = split_cos(
        (big[0][:, None, :], big[1][:, None, :]), (small[0][None], small[1][None])
    ).reshape(length, length)
    weight = jnp.where((mode == 0) | (mode == length // 2), 1.0, 2.0) / float(length * length)
    big = turn_phase(mode[:, None] * hi[None, :], length)
    small = turn_phase(mode[:, None] * lo[None, :] + shift[:, None], length)
    inverse = split_cos(
        (big[0][:, :, None], big[1][:, :, None]), (small[0][:, None, :], small[1][:, None, :])
    ).reshape(length, length)
    inverse = weight[:, None] * inverse
    return lax.optimization_barrier((forward, inverse))


def column_table(length):
    fine, coarse = grid_split(length)
    hi = lax.optimization_barrier(jnp.arange(coarse, dtype=jnp.int32)) * fine
    lo = lax.optimization_barrier(jnp.arange(fine, dtype=jnp.int32))
    n = lax.optimization_barrier(jnp.arange(length, dtype=jnp.int32))
    big = turn_phase(hi[:, None] * n[None, :], length)
    small = turn_phase(lo[:, None] * n[None, :], length)
    big = (big[0][:, None, :], big[1][:, None, :])
    small = (small[0][None], small[1][None])
    cosine = split_cos(big, small).reshape(length, length)
    sine = split_sin(big, small).reshape(length, length)
    return lax.optimization_barrier(jnp.concatenate([cosine, sine], axis=1))


def wave_tables(modes, length):
    signed = jnp.where(modes >= length // 2, modes - length, modes)
    wavenumber = 2.0 * math.pi / length * signed.astype(jnp.float32)
    slope = jnp.where(modes == length // 2, jnp.zeros_like(wavenumber), wavenumber)
    retained = jnp.where(3 * jnp.abs(signed) < length, 1.0, 0.0).astype(jnp.float32)
    return (wavenumber, slope, retained)


def fetch_parent(vorticity, ancestors):
    high = lax.axis_size("ph")
    low = lax.axis_size("pl")
    my_high = lax.axis_index("ph")
    my_low = lax.axis_index("pl")
    held = lax.all_gather(vorticity, "pl", axis=0, tiled=True)
    forwarded = []
    for step in range(1, high):
        target = ((my_high + step) % high) * low + my_low
        need = ancestors[target]
        chosen = lax.dynamic_index_in_dim(held, need % low, axis=0, keepdims=True)
        perm = [(i, (i + step) % high) for i in range(high)]
        forwarded.append(lax.ppermute(chosen, "ph", perm))
    candidates = jnp.concatenate([held] + forwarded, axis=0)
    need = ancestors[my_high * low + my_low]
    need_high, need_low = need // low, need % low
    index = jnp.where(need_high == my_high, need_low, low + (my_high - need_high) % high - 1)
    return lax.dynamic_index_in_dim(candidates, index, axis=0, keepdims=True)


def local(vorticity, ancestors, noise):
    particle_count, row_count, length = vorticity.shape
    parts = lax.axis_size("field")
    half = length // (2 * parts)
    me = lax.axis_index("field")

    row_fwd, row_inv = row_tables(length, parts)
    col_cs = column_table(length)

    slot = jnp.arange(half + 1, dtype=jnp.int32)
    mode_x = jnp.where(slot < half, half * me + slot, length // 2)
    mode_y = jnp.arange(length, dtype=jnp.int32)
    wave_x, slope_x, kept_x = wave_tables(mode_x, length)
    wave_y, slope_y, kept_y = wave_tables(mode_y, length)
    squared = wave_x[:, None] ** 2 + wave_y[None, :] ** 2
    inverse_sq = jnp.where(squared > 0, 1.0 / jnp.where(squared > 0, squared, 1.0), 0.0)
    dealias = kept_x[:, None] * kept_y[None, :]
    spectrum_weight = 1.0 / (1.0 + squared)
    slope_x = slope_x[:, None]
    slope_y = slope_y[None, :]
    on_first = me == 0
    pair_mask = jnp.where(on_first & (slot[:half] == 0), 0.0, 1.0)[:, None]
    nyquist_gate = jnp.where(on_first, 1.0, 0.0)

    def forward(fields):
        batch = fields.shape[0]
        rows = jnp.einsum("byx,xo->byo", fields, row_fwd, precision=HIGHEST)
        rows = rows.reshape(batch, row_count, parts, 2 * half)
        cols = lax.all_to_all(rows, "field", split_axis=2, concat_axis=1, tiled=True)
        cols = cols.reshape(batch, length, 2 * half)
        prod = jnp.einsum("byt,yk->btk", cols, col_cs, precision=HIGHEST)
        pc = prod[:, :, :length]
        ps = prod[:, :, length:]
        real = pc[:, :half] + pair_mask * ps[:, half:]
        imag = pair_mask * pc[:, half:] - ps[:, :half]
        ny_real = nyquist_gate * pc[:, half : half + 1]
        ny_imag = -nyquist_gate * ps[:, half : half + 1]
        real = jnp.concatenate([real, ny_real], axis=1)
        imag = jnp.concatenate([imag, ny_imag], axis=1)
        return real, imag

    def inverse(real, imag):
        batch = real.shape[0]
        stacked = jnp.concatenate([real, imag], axis=1)
        prod = jnp.einsum("bjm,mk->bjk", stacked, col_cs, precision=HIGHEST)
        n_slot = half + 1
        wr_c = prod[:, :n_slot, :length]
        wr_s = prod[:, :n_slot, length:]
        wi_c = prod[:, n_slot:, :length]
        wi_s = prod[:, n_slot:, length:]
        z_real = wr_c - wi_s
        z_imag = wr_s + wi_c
        first_imag = jnp.where(on_first, z_real[:, half : half + 1], z_imag[:, 0:1])
        send = jnp.concatenate([z_real[:, :half], first_imag, z_imag[:, 1:half]], axis=1)
        send = send.reshape(batch, 2 * half, parts, row_count)
        back = lax.all_to_all(send, "field", split_axis=2, concat_axis=1, tiled=True)
        back = back.reshape(batch, length, row_count)
        return jnp.einsum("bsy,sx->byx", back, row_inv, precision=HIGHEST)

    def tendency(real, imag):
        pot_r = real * inverse_sq
        pot_i = imag * inverse_sq
        fr = jnp.stack(
            [
                -slope_y * pot_i,
                slope_x * pot_i,
                -slope_x * imag,
                -slope_y * imag,
            ],
            axis=0,
        )
        fi = jnp.stack(
            [
                slope_y * pot_r,
                -slope_x * pot_r,
                slope_x * real,
                slope_y * real,
            ],
            axis=0,
        )
        physical = inverse(fr, fi)
        advection = physical[0:1] * physical[2:3] + physical[1:2] * physical[3:4]
        ar, ai = forward(advection)
        return (
            -dealias * ar[0] - VISCOSITY * squared * real,
            -dealias * ai[0] - VISCOSITY * squared * imag,
        )

    noise_r, noise_i = forward(noise.astype(jnp.float32))
    parents = fetch_parent(vorticity, ancestors).astype(jnp.float32)
    par_r, par_i = forward(parents)

    prop_r = PARENT_WEIGHT * par_r[0] + NOISE_WEIGHT * spectrum_weight * noise_r[0]
    prop_i = PARENT_WEIGHT * par_i[0] + NOISE_WEIGHT * spectrum_weight * noise_i[0]
    rate1_r, rate1_i = tendency(prop_r, prop_i)
    mid_r = prop_r + TIME_STEP * rate1_r
    mid_i = prop_i + TIME_STEP * rate1_i
    rate2_r, rate2_i = tendency(mid_r, mid_i)
    fin_r = prop_r + 0.5 * TIME_STEP * (rate1_r + rate2_r)
    fin_i = prop_i + 0.5 * TIME_STEP * (rate1_i + rate2_i)
    return inverse(fin_r[None], fin_i[None])


def split_particles(mesh):
    count = mesh.shape["particle"]
    low = 1 << ((count.bit_length() - 1) // 2)
    while count % low:
        low //= 2
    devices = mesh.devices.reshape(count // low, low, mesh.shape["field"])
    return Mesh(devices, ("ph", "pl", "field"))


def solution(mesh):
    split = split_particles(mesh)
    placed = P(("ph", "pl"), "field", None)
    return jax.shard_map(
        local, mesh=split, in_specs=(placed, P(), placed), out_specs=placed, check_vma=False
    )
```

```python
import math

import jax
import jax.numpy as jnp
from jax import lax
from jax.sharding import PartitionSpec as P

PARENT_WEIGHT = 0.8
NOISE_WEIGHT = 0.6
VISCOSITY = 0.05
TIME_STEP = 0.1
HIGHEST = lax.Precision.HIGH


def turn_phase(turns, length):
    reduced = turns % length
    reduced = jnp.where(reduced >= length // 2, reduced - length, reduced)
    angle = (2.0 * math.pi / length) * reduced.astype(jnp.float32)
    return jnp.cos(angle), jnp.sin(angle)


def split_cos(coarse, fine):
    return coarse[0] * fine[0] - coarse[1] * fine[1]


def split_sin(coarse, fine):
    return coarse[1] * fine[0] + coarse[0] * fine[1]


def slot_modes(length, parts):
    half = length // (2 * parts)
    order = lax.optimization_barrier(jnp.arange(length, dtype=jnp.int32))
    dest = order // (2 * half)
    t = order % (2 * half)
    mode = half * dest + t % half
    nyquist = order == half
    mode = jnp.where(nyquist, length // 2, mode)
    use_cos = (t < half) | nyquist
    return mode, use_cos


def grid_split(length):
    fine = 1 << ((length.bit_length() - 1) // 2)
    return fine, length // fine


def row_tables(length, parts):
    mode, use_cos = slot_modes(length, parts)
    fine, coarse = grid_split(length)
    hi = lax.optimization_barrier(jnp.arange(coarse, dtype=jnp.int32)) * fine
    lo = lax.optimization_barrier(jnp.arange(fine, dtype=jnp.int32))
    shift = jnp.where(use_cos, 0, length // 4)
    big = turn_phase(hi[:, None] * mode[None, :], length)
    small = turn_phase(lo[:, None] * mode[None, :] + shift[None, :], length)
    forward = split_cos(
        (big[0][:, None, :], big[1][:, None, :]), (small[0][None], small[1][None])
    ).reshape(length, length)
    weight = jnp.where((mode == 0) | (mode == length // 2), 1.0, 2.0) / float(length * length)
    big = turn_phase(mode[:, None] * hi[None, :], length)
    small = turn_phase(mode[:, None] * lo[None, :] + shift[:, None], length)
    inverse = split_cos(
        (big[0][:, :, None], big[1][:, :, None]), (small[0][:, None, :], small[1][:, None, :])
    ).reshape(length, length)
    return lax.optimization_barrier((inverse, weight[None, :] * forward))


def column_table(length):
    fine, coarse = grid_split(length)
    hi = lax.optimization_barrier(jnp.arange(coarse, dtype=jnp.int32)) * fine
    lo = lax.optimization_barrier(jnp.arange(fine, dtype=jnp.int32))
    n = lax.optimization_barrier(jnp.arange(length, dtype=jnp.int32))
    big = turn_phase(hi[:, None] * n[None, :], length)
    small = turn_phase(lo[:, None] * n[None, :], length)
    big = (big[0][:, None, :], big[1][:, None, :])
    small = (small[0][None], small[1][None])
    cosine = split_cos(big, small).reshape(length, length)
    sine = split_sin(big, small).reshape(length, length)
    return lax.optimization_barrier(jnp.concatenate([cosine, sine], axis=0))


def wave_tables(modes, length):
    signed = jnp.where(modes >= length // 2, modes - length, modes)
    wavenumber = 2.0 * math.pi / length * signed.astype(jnp.float32)
    slope = jnp.where(modes == length // 2, jnp.zeros_like(wavenumber), wavenumber)
    retained = jnp.where(3 * jnp.abs(signed) < length, 1.0, 0.0).astype(jnp.float32)
    return (wavenumber, slope, retained)


def local(vorticity, ancestors, noise):
    particle_count, row_count, length = vorticity.shape
    parts = lax.axis_size("field")
    half = length // (2 * parts)
    me = lax.axis_index("field")
    first_particle = lax.axis_index("particle") * particle_count

    row_fwd, row_inv = row_tables(length, parts)
    col_cs = column_table(length)

    slot = jnp.arange(half + 1, dtype=jnp.int32)
    mode_x = jnp.where(slot < half, half * me + slot, length // 2)
    mode_y = jnp.arange(length, dtype=jnp.int32)
    wave_x, slope_x, kept_x = wave_tables(mode_x, length)
    wave_y, slope_y, kept_y = wave_tables(mode_y, length)
    squared = wave_x[None, :] ** 2 + wave_y[:, None] ** 2
    inverse_sq = jnp.where(squared > 0, 1.0 / jnp.where(squared > 0, squared, 1.0), 0.0)
    dealias = kept_x[None, :] * kept_y[:, None]
    spectrum_weight = 1.0 / (1.0 + squared)
    slope_x = slope_x[None, :]
    slope_y = slope_y[:, None]
    on_first = me == 0
    pair_mask = jnp.where(on_first & (slot[:half] == 0), 0.0, 1.0)[None, :]
    nyquist_gate = jnp.where(on_first, 1.0, 0.0)

    def forward(field_t):
        rows = jnp.einsum("ox,xy->oy", row_fwd, field_t, precision=HIGHEST)
        rows = rows.reshape(parts, 2 * half, row_count)
        cols = lax.all_to_all(rows, "field", split_axis=0, concat_axis=0, tiled=True)
        cols = jnp.swapaxes(cols, 1, 2).reshape(length, 2 * half)
        prod = jnp.einsum("ky,yt->kt", col_cs, cols, precision=HIGHEST)
        pc = prod[:length]
        ps = prod[length:]
        real = pc[:, :half] + pair_mask * ps[:, half:]
        imag = pair_mask * pc[:, half:] - ps[:, :half]
        ny_real = nyquist_gate * pc[:, half : half + 1]
        ny_imag = -nyquist_gate * ps[:, half : half + 1]
        real = jnp.concatenate([real, ny_real], axis=1)
        imag = jnp.concatenate([imag, ny_imag], axis=1)
        return real, imag

    def inverse(real, imag):
        batch = real.shape[0]
        n_slot = half + 1
        stacked = jnp.concatenate([real, imag], axis=2)
        stacked = jnp.swapaxes(stacked, 0, 1).reshape(length, batch * 2 * n_slot)
        prod = jnp.einsum("km,mn->kn", col_cs, stacked, precision=HIGHEST)
        prod = prod.reshape(2 * length, batch, 2 * n_slot)
        wr_c = prod[:length, :, :n_slot]
        wi_c = prod[:length, :, n_slot:]
        wr_s = prod[length:, :, :n_slot]
        wi_s = prod[length:, :, n_slot:]
        z_real = wr_c - wi_s
        z_imag = wr_s + wi_c
        first_imag = jnp.where(on_first, z_real[:, :, half : half + 1], z_imag[:, :, 0:1])
        send = jnp.concatenate([z_real[:, :, :half], first_imag, z_imag[:, :, 1:half]], axis=2)
        send = send.reshape(parts, row_count, batch, 2 * half)
        back = lax.all_to_all(send, "field", split_axis=0, concat_axis=0, tiled=True)
        back = jnp.transpose(back, (0, 3, 2, 1)).reshape(length, batch * row_count)
        out = jnp.einsum("xs,sn->xn", row_inv, back, precision=HIGHEST)
        return out.reshape(length, batch, row_count)

    def tendency(real, imag):
        pot_r = real * inverse_sq
        pot_i = imag * inverse_sq
        fr = jnp.stack(
            [
                -slope_y * pot_i,
                slope_x * pot_i,
                -slope_x * imag,
                -slope_y * imag,
            ],
            axis=0,
        )
        fi = jnp.stack(
            [
                slope_y * pot_r,
                -slope_x * pot_r,
                slope_x * real,
                slope_y * real,
            ],
            axis=0,
        )
        physical = inverse(fr, fi)
        advection = physical[:, 0] * physical[:, 2] + physical[:, 1] * physical[:, 3]
        ar, ai = forward(advection)
        return (
            -dealias * ar - VISCOSITY * squared * real,
            -dealias * ai - VISCOSITY * squared * imag,
        )

    noise_r, noise_i = forward(noise[0].astype(jnp.float32).T)
    shard_rows = lax.all_gather(vorticity, "particle", axis=0, tiled=True)
    wanted = lax.dynamic_slice_in_dim(ancestors, first_particle, particle_count)
    parents = jnp.take(shard_rows, wanted, axis=0).astype(jnp.float32)
    par_r, par_i = forward(parents[0].T)

    prop_r = PARENT_WEIGHT * par_r + NOISE_WEIGHT * spectrum_weight * noise_r
    prop_i = PARENT_WEIGHT * par_i + NOISE_WEIGHT * spectrum_weight * noise_i
    rate1_r, rate1_i = tendency(prop_r, prop_i)
    mid_r = prop_r + TIME_STEP * rate1_r
    mid_i = prop_i + TIME_STEP * rate1_i
    rate2_r, rate2_i = tendency(mid_r, mid_i)
    fin_r = prop_r + 0.5 * TIME_STEP * (rate1_r + rate2_r)
    fin_i = prop_i + 0.5 * TIME_STEP * (rate1_i + rate2_i)
    out = inverse(fin_r[None], fin_i[None])
    return jnp.transpose(out, (1, 2, 0))


def solution(mesh):
    placed = (P("particle", "field", None), P(), P("particle", "field", None))
    return jax.shard_map(
        local, mesh=mesh, in_specs=placed, out_specs=P("particle", "field", None), check_vma=False
    )
```

```python
import math

import jax
import jax.numpy as jnp
from jax import lax
from jax.sharding import PartitionSpec as P

PARENT_WEIGHT = 0.8
NOISE_WEIGHT = 0.6
VISCOSITY = 0.05
TIME_STEP = 0.1
HIGHEST = lax.Precision.HIGH


def turn_phase(turns, length):
    reduced = turns % length
    reduced = jnp.where(reduced >= length // 2, reduced - length, reduced)
    angle = (2.0 * math.pi / length) * reduced.astype(jnp.float32)
    return jnp.cos(angle), jnp.sin(angle)


def split_cos(coarse, fine):
    return coarse[0] * fine[0] - coarse[1] * fine[1]


def split_sin(coarse, fine):
    return coarse[1] * fine[0] + coarse[0] * fine[1]


def slot_modes(length, parts):
    half = length // (2 * parts)
    order = lax.optimization_barrier(jnp.arange(length, dtype=jnp.int32))
    dest = order // (2 * half)
    t = order % (2 * half)
    mode = half * dest + t % half
    nyquist = order == half
    mode = jnp.where(nyquist, length // 2, mode)
    use_cos = (t < half) | nyquist
    return mode, use_cos


def grid_split(length):
    fine = 1 << ((length.bit_length() - 1) // 2)
    return fine, length // fine


def row_tables(length, parts):
    mode, use_cos = slot_modes(length, parts)
    fine, coarse = grid_split(length)
    hi = lax.optimization_barrier(jnp.arange(coarse, dtype=jnp.int32)) * fine
    lo = lax.optimization_barrier(jnp.arange(fine, dtype=jnp.int32))
    shift = jnp.where(use_cos, 0, length // 4)
    big = turn_phase(hi[:, None] * mode[None, :], length)
    small = turn_phase(lo[:, None] * mode[None, :] + shift[None, :], length)
    forward = split_cos(
        (big[0][:, None, :], big[1][:, None, :]), (small[0][None], small[1][None])
    ).reshape(length, length)
    weight = jnp.where((mode == 0) | (mode == length // 2), 1.0, 2.0) / float(length * length)
    big = turn_phase(mode[:, None] * hi[None, :], length)
    small = turn_phase(mode[:, None] * lo[None, :] + shift[:, None], length)
    inverse = split_cos(
        (big[0][:, :, None], big[1][:, :, None]), (small[0][:, None, :], small[1][:, None, :])
    ).reshape(length, length)
    return lax.optimization_barrier((inverse, weight[None, :] * forward))


def column_tables(length):
    fine, coarse = grid_split(length)
    hi = lax.optimization_barrier(jnp.arange(coarse, dtype=jnp.int32)) * fine
    lo = lax.optimization_barrier(jnp.arange(fine, dtype=jnp.int32))
    r = lax.optimization_barrier(jnp.arange(length, dtype=jnp.int32))
    folded = r > length // 2
    rmode = jnp.where(folded, r - length // 2, r)
    shift = jnp.where(folded, -(length // 4), 0)
    big = turn_phase(rmode[:, None] * hi[None, :], length)
    small = turn_phase(rmode[:, None] * lo[None, :] + shift[:, None], length)
    forward = split_cos(
        (big[0][:, :, None], big[1][:, :, None]), (small[0][:, None, :], small[1][:, None, :])
    ).reshape(length, length)
    big = turn_phase(hi[:, None] * rmode[None, :], length)
    small = turn_phase(lo[:, None] * rmode[None, :] + shift[None, :], length)
    inverse = split_cos(
        (big[0][:, None, :], big[1][:, None, :]), (small[0][None], small[1][None])
    ).reshape(length, length)
    return lax.optimization_barrier((forward, inverse))


def wave_tables(modes, length):
    signed = jnp.where(modes >= length // 2, modes - length, modes)
    wavenumber = 2.0 * math.pi / length * signed.astype(jnp.float32)
    slope = jnp.where(modes == length // 2, jnp.zeros_like(wavenumber), wavenumber)
    retained = jnp.where(3 * jnp.abs(signed) < length, 1.0, 0.0).astype(jnp.float32)
    return (wavenumber, slope, retained)


def local(vorticity, ancestors, noise):
    particle_count, row_count, length = vorticity.shape
    parts = lax.axis_size("field")
    half = length // (2 * parts)
    me = lax.axis_index("field")
    first_particle = lax.axis_index("particle") * particle_count

    row_fwd, row_inv = row_tables(length, parts)
    col_fwd, col_inv = column_tables(length)
    mid = length // 2

    slot = jnp.arange(half + 1, dtype=jnp.int32)
    mode_x = jnp.where(slot < half, half * me + slot, length // 2)
    position_y = jnp.arange(length, dtype=jnp.int32)
    mode_y = jnp.where(position_y > length // 2, length + length // 2 - position_y, position_y)
    wave_x, slope_x, kept_x = wave_tables(mode_x, length)
    wave_y, slope_y, kept_y = wave_tables(mode_y, length)
    squared = wave_x[None, :] ** 2 + wave_y[:, None] ** 2
    inverse_sq = jnp.where(squared > 0, 1.0 / jnp.where(squared > 0, squared, 1.0), 0.0)
    dealias = kept_x[None, :] * kept_y[:, None]
    spectrum_weight = 1.0 / (1.0 + squared)
    slope_x = slope_x[None, :]
    slope_y = slope_y[:, None]
    on_first = me == 0
    pair_mask = jnp.where(on_first & (slot[:half] == 0), 0.0, 1.0)[None, :]
    nyquist_gate = jnp.where(on_first, 1.0, 0.0)

    def forward(field_t):
        rows = jnp.einsum("ox,xy->oy", row_fwd, field_t, precision=HIGHEST)
        rows = rows.reshape(parts, 2 * half, row_count)
        cols = lax.all_to_all(rows, "field", split_axis=0, concat_axis=0, tiled=True)
        cols = jnp.swapaxes(cols, 1, 2).reshape(length, 2 * half)
        prod = jnp.einsum("ry,yt->rt", col_fwd, cols, precision=HIGHEST)
        pc = prod[: mid + 1]
        ps = prod[mid + 1 :]
        ps_ext = jnp.pad(ps, ((1, 1), (0, 0)))
        real_a = pc[:, :half] + pair_mask * ps_ext[:, half:]
        imag_a = pair_mask * pc[:, half:] - ps_ext[:, :half]
        real_b = pc[1:mid, :half] - pair_mask * ps[:, half:]
        imag_b = pair_mask * pc[1:mid, half:] + ps[:, :half]
        ny_real = nyquist_gate * jnp.concatenate([pc[:, half : half + 1], pc[1:mid, half : half + 1]], axis=0)
        ny_imag = nyquist_gate * jnp.concatenate([-ps_ext[:, half : half + 1], ps[:, half : half + 1]], axis=0)
        real = jnp.concatenate([jnp.concatenate([real_a, real_b], axis=0), ny_real], axis=1)
        imag = jnp.concatenate([jnp.concatenate([imag_a, imag_b], axis=0), ny_imag], axis=1)
        return real, imag

    def inverse(real, imag):
        batch = real.shape[0]
        n_slot = half + 1

        def plus(w):
            return jnp.concatenate([w[:, :1], w[:, 1:mid] + w[:, mid + 1 :], w[:, mid : mid + 1]], axis=1)

        def minus(w):
            return w[:, 1:mid] - w[:, mid + 1 :]

        v_real = jnp.concatenate([plus(real), -minus(imag)], axis=1)
        v_imag = jnp.concatenate([plus(imag), minus(real)], axis=1)
        stacked = jnp.concatenate([v_real, v_imag], axis=2)
        stacked = jnp.swapaxes(stacked, 0, 1).reshape(length, batch * 2 * n_slot)
        prod = jnp.einsum("yr,rn->yn", col_inv, stacked, precision=HIGHEST)
        prod = prod.reshape(length, batch, 2 * n_slot)
        z_real = prod[:, :, :n_slot]
        z_imag = prod[:, :, n_slot:]
        first_imag = jnp.where(on_first, z_real[:, :, half : half + 1], z_imag[:, :, 0:1])
        send = jnp.concatenate([z_real[:, :, :half], first_imag, z_imag[:, :, 1:half]], axis=2)
        send = send.reshape(parts, row_count, batch, 2 * half)
        back = lax.all_to_all(send, "field", split_axis=0, concat_axis=0, tiled=True)
        back = jnp.transpose(back, (0, 3, 2, 1)).reshape(length, batch * row_count)
        out = jnp.einsum("xs,sn->xn", row_inv, back, precision=HIGHEST)
        return out.reshape(length, batch, row_count)

    def tendency(real, imag):
        pot_r = real * inverse_sq
        pot_i = imag * inverse_sq
        fr = jnp.stack(
            [
                -slope_y * pot_i,
                slope_x * pot_i,
                -slope_x * imag,
                -slope_y * imag,
            ],
            axis=0,
        )
        fi = jnp.stack(
            [
                slope_y * pot_r,
                -slope_x * pot_r,
                slope_x * real,
                slope_y * real,
            ],
            axis=0,
        )
        physical = inverse(fr, fi)
        advection = physical[:, 0] * physical[:, 2] + physical[:, 1] * physical[:, 3]
        ar, ai = forward(advection)
        return (
            -dealias * ar - VISCOSITY * squared * real,
            -dealias * ai - VISCOSITY * squared * imag,
        )

    noise_r, noise_i = forward(noise[0].astype(jnp.float32).T)
    shard_rows = lax.all_gather(vorticity, "particle", axis=0, tiled=True)
    wanted = lax.dynamic_slice_in_dim(ancestors, first_particle, particle_count)
    parents = jnp.take(shard_rows, wanted, axis=0).astype(jnp.float32)
    par_r, par_i = forward(parents[0].T)

    prop_r = PARENT_WEIGHT * par_r + NOISE_WEIGHT * spectrum_weight * noise_r
    prop_i = PARENT_WEIGHT * par_i + NOISE_WEIGHT * spectrum_weight * noise_i
    rate1_r, rate1_i = tendency(prop_r, prop_i)
    mid_r = prop_r + TIME_STEP * rate1_r
    mid_i = prop_i + TIME_STEP * rate1_i
    rate2_r, rate2_i = tendency(mid_r, mid_i)
    fin_r = prop_r + 0.5 * TIME_STEP * (rate1_r + rate2_r)
    fin_i = prop_i + 0.5 * TIME_STEP * (rate1_i + rate2_i)
    out = inverse(fin_r[None], fin_i[None])
    return jnp.transpose(out, (1, 2, 0))


def solution(mesh):
    placed = (P("particle", "field", None), P(), P("particle", "field", None))
    return jax.shard_map(
        local, mesh=mesh, in_specs=placed, out_specs=P("particle", "field", None), check_vma=False
    )
```

```python
import math

import jax
import jax.numpy as jnp
from jax import lax
from jax.sharding import PartitionSpec as P

PARENT_WEIGHT = 0.8
NOISE_WEIGHT = 0.6
VISCOSITY = 0.05
TIME_STEP = 0.1
HIGHEST = lax.Precision.HIGH


def turn_phase(turns, length):
    reduced = turns % length
    reduced = jnp.where(reduced >= length // 2, reduced - length, reduced)
    angle = (2.0 * math.pi / length) * reduced.astype(jnp.float32)
    return jnp.cos(angle), jnp.sin(angle)


def split_cos(coarse, fine):
    return coarse[0] * fine[0] - coarse[1] * fine[1]


def split_sin(coarse, fine):
    return coarse[1] * fine[0] + coarse[0] * fine[1]


def slot_modes(length, parts):
    half = length // (2 * parts)
    order = lax.optimization_barrier(jnp.arange(length, dtype=jnp.int32))
    dest = order // (2 * half)
    t = order % (2 * half)
    mode = half * dest + t % half
    nyquist = order == half
    mode = jnp.where(nyquist, length // 2, mode)
    use_cos = (t < half) | nyquist
    return mode, use_cos


def grid_split(length):
    fine = 1 << ((length.bit_length() - 1) // 2)
    return fine, length // fine


def phase_table(row_turns, row_shift, length):
    fine, coarse = grid_split(length)
    hi = lax.optimization_barrier(jnp.arange(coarse, dtype=jnp.int32)) * fine
    lo = lax.optimization_barrier(jnp.arange(fine, dtype=jnp.int32))
    big = turn_phase(row_turns[:, None] * hi[None, :], length)
    small = turn_phase(row_turns[:, None] * lo[None, :] + row_shift[:, None], length)
    table = split_cos(
        (big[0][:, :, None], big[1][:, :, None]), (small[0][:, None, :], small[1][:, None, :])
    )
    return table.reshape(row_turns.shape[0], length)


def row_tables(length, parts):
    half = length // (2 * parts)
    mid = length // 2
    dest = lax.optimization_barrier(jnp.arange(parts * half, dtype=jnp.int32))
    mode = (dest // half) * half + dest % half
    zero = jnp.zeros_like(mode)
    weight = jnp.where(mode == 0, 1.0, 2.0) / float(length * length)
    cosine = phase_table(mode, zero, length)
    sine = phase_table(mode, zero + length // 4, length)
    fwd_cos = cosine[:, : mid + 1]
    fwd_sin = sine[:, 1:mid]
    inv_cos = weight[None, :] * fwd_cos.T
    inv_sin = weight[None, :] * fwd_sin.T
    return lax.optimization_barrier((fwd_cos, fwd_sin, inv_cos, inv_sin))


def column_tables(length):
    fine, coarse = grid_split(length)
    hi = lax.optimization_barrier(jnp.arange(coarse, dtype=jnp.int32)) * fine
    lo = lax.optimization_barrier(jnp.arange(fine, dtype=jnp.int32))
    r = lax.optimization_barrier(jnp.arange(length, dtype=jnp.int32))
    folded = r > length // 2
    rmode = jnp.where(folded, r - length // 2, r)
    shift = jnp.where(folded, -(length // 4), 0)
    big = turn_phase(rmode[:, None] * hi[None, :], length)
    small = turn_phase(rmode[:, None] * lo[None, :] + shift[:, None], length)
    forward = split_cos(
        (big[0][:, :, None], big[1][:, :, None]), (small[0][:, None, :], small[1][:, None, :])
    ).reshape(length, length)
    big = turn_phase(hi[:, None] * rmode[None, :], length)
    small = turn_phase(lo[:, None] * rmode[None, :] + shift[None, :], length)
    inverse = split_cos(
        (big[0][:, None, :], big[1][:, None, :]), (small[0][None], small[1][None])
    ).reshape(length, length)
    return lax.optimization_barrier((forward, inverse))


def wave_tables(modes, length):
    signed = jnp.where(modes >= length // 2, modes - length, modes)
    wavenumber = 2.0 * math.pi / length * signed.astype(jnp.float32)
    slope = jnp.where(modes == length // 2, jnp.zeros_like(wavenumber), wavenumber)
    retained = jnp.where(3 * jnp.abs(signed) < length, 1.0, 0.0).astype(jnp.float32)
    return (wavenumber, slope, retained)


def local(vorticity, ancestors, noise):
    particle_count, row_count, length = vorticity.shape
    parts = lax.axis_size("field")
    half = length // (2 * parts)
    me = lax.axis_index("field")
    first_particle = lax.axis_index("particle") * particle_count

    fwd_cos, fwd_sin, inv_cos, inv_sin = row_tables(length, parts)
    col_fwd, col_inv = column_tables(length)
    mid = length // 2

    slot = jnp.arange(half + 1, dtype=jnp.int32)
    mode_x = jnp.where(slot < half, half * me + slot, length // 2)
    position_y = jnp.arange(length, dtype=jnp.int32)
    mode_y = jnp.where(position_y > length // 2, length + length // 2 - position_y, position_y)
    wave_x, slope_x, kept_x = wave_tables(mode_x, length)
    wave_y, slope_y, kept_y = wave_tables(mode_y, length)
    squared = wave_x[None, :] ** 2 + wave_y[:, None] ** 2
    inverse_sq = jnp.where(squared > 0, 1.0 / jnp.where(squared > 0, squared, 1.0), 0.0)
    dealias = kept_x[None, :] * kept_y[:, None]
    spectrum_weight = 1.0 / (1.0 + squared)
    slope_x = slope_x[None, :]
    slope_y = slope_y[:, None]
    on_first = me == 0
    pair_mask = jnp.where(on_first & (slot[:half] == 0), 0.0, 1.0)[None, :]
    nyquist_gate = jnp.where(on_first, 1.0, 0.0)

    position_x = jnp.arange(length, dtype=jnp.int32)
    alternate = jnp.where(position_x % 2 == 0, 1.0, -1.0)

    def fold(field_t):
        return jnp.concatenate([field_t[: mid + 1], field_t[mid + 1 :][::-1]], axis=0)

    def forward(field_t):
        plus = jnp.concatenate(
            [field_t[:1], field_t[1:mid] + field_t[mid + 1 :], field_t[mid : mid + 1]], axis=0
        )
        minus = field_t[1:mid] - field_t[mid + 1 :]
        rows_cos = jnp.einsum("ox,xy->oy", fwd_cos, plus, precision=HIGHEST)
        rows_sin = jnp.einsum("ox,xy->oy", fwd_sin, minus, precision=HIGHEST)
        nyquist = jnp.einsum("x,xy->y", alternate, field_t, precision=HIGHEST)
        rows_sin = rows_sin.reshape(parts, half, row_count)
        rows_sin = rows_sin.at[0, 0].set(nyquist)
        rows = jnp.concatenate([rows_cos.reshape(parts, half, row_count), rows_sin], axis=1)
        cols = lax.all_to_all(rows, "field", split_axis=0, concat_axis=0, tiled=True)
        cols = jnp.swapaxes(cols, 1, 2).reshape(length, 2 * half)
        prod = jnp.einsum("ry,yt->rt", col_fwd, cols, precision=HIGHEST)
        pc = prod[: mid + 1]
        ps = prod[mid + 1 :]
        ps_ext = jnp.pad(ps, ((1, 1), (0, 0)))
        real_a = pc[:, :half] + pair_mask * ps_ext[:, half:]
        imag_a = pair_mask * pc[:, half:] - ps_ext[:, :half]
        real_b = pc[1:mid, :half] - pair_mask * ps[:, half:]
        imag_b = pair_mask * pc[1:mid, half:] + ps[:, :half]
        ny_real = nyquist_gate * jnp.concatenate([pc[:, half : half + 1], pc[1:mid, half : half + 1]], axis=0)
        ny_imag = nyquist_gate * jnp.concatenate([-ps_ext[:, half : half + 1], ps[:, half : half + 1]], axis=0)
        real = jnp.concatenate([jnp.concatenate([real_a, real_b], axis=0), ny_real], axis=1)
        imag = jnp.concatenate([jnp.concatenate([imag_a, imag_b], axis=0), ny_imag], axis=1)
        return real, imag

    def inverse(real, imag):
        batch = real.shape[0]
        n_slot = half + 1

        def plus(w):
            return jnp.concatenate([w[:, :1], w[:, 1:mid] + w[:, mid + 1 :], w[:, mid : mid + 1]], axis=1)

        def minus(w):
            return w[:, 1:mid] - w[:, mid + 1 :]

        v_real = jnp.concatenate([plus(real), -minus(imag)], axis=1)
        v_imag = jnp.concatenate([plus(imag), minus(real)], axis=1)
        stacked = jnp.concatenate([v_real, v_imag], axis=2)
        stacked = jnp.swapaxes(stacked, 0, 1).reshape(length, batch * 2 * n_slot)
        prod = jnp.einsum("yr,rn->yn", col_inv, stacked, precision=HIGHEST)
        prod = prod.reshape(length, batch, 2 * n_slot)
        z_real = prod[:, :, :n_slot]
        z_imag = prod[:, :, n_slot:]
        first_imag = jnp.where(on_first, z_real[:, :, half : half + 1], z_imag[:, :, 0:1])
        send = jnp.concatenate([z_real[:, :, :half], first_imag, z_imag[:, :, 1:half]], axis=2)
        send = send.reshape(parts, row_count, batch, 2 * half)
        back = lax.all_to_all(send, "field", split_axis=0, concat_axis=0, tiled=True)
        back = jnp.transpose(back, (0, 3, 2, 1)).reshape(parts, 2 * half, batch * row_count)
        back_cos = back[:, :half].reshape(parts * half, batch * row_count)
        back_sin = back[:, half:].reshape(parts * half, batch * row_count)
        nyquist = back[0, half] / float(length * length)
        out_cos = jnp.einsum("xs,sn->xn", inv_cos, back_cos, precision=HIGHEST)
        out_sin = jnp.einsum("xs,sn->xn", inv_sin, back_sin, precision=HIGHEST)
        out_sin_ext = jnp.pad(out_sin, ((1, 1), (0, 0)))
        out = jnp.concatenate([out_cos + out_sin_ext, out_cos[1:mid] - out_sin], axis=0)
        out = out + alternate[:, None] * nyquist[None, :]
        return out.reshape(length, batch, row_count)

    def tendency(real, imag):
        pot_r = real * inverse_sq
        pot_i = imag * inverse_sq
        fr = jnp.stack(
            [
                -slope_y * pot_i,
                slope_x * pot_i,
                -slope_x * imag,
                -slope_y * imag,
            ],
            axis=0,
        )
        fi = jnp.stack(
            [
                slope_y * pot_r,
                -slope_x * pot_r,
                slope_x * real,
                slope_y * real,
            ],
            axis=0,
        )
        physical = inverse(fr, fi)
        advection = physical[:, 0] * physical[:, 2] + physical[:, 1] * physical[:, 3]
        ar, ai = forward(advection)
        return (
            -dealias * ar - VISCOSITY * squared * real,
            -dealias * ai - VISCOSITY * squared * imag,
        )

    noise_r, noise_i = forward(fold(noise[0].astype(jnp.float32).T))
    shard_rows = lax.all_gather(vorticity, "particle", axis=0, tiled=True)
    wanted = lax.dynamic_slice_in_dim(ancestors, first_particle, particle_count)
    parents = jnp.take(shard_rows, wanted, axis=0).astype(jnp.float32)
    par_r, par_i = forward(fold(parents[0].T))

    prop_r = PARENT_WEIGHT * par_r + NOISE_WEIGHT * spectrum_weight * noise_r
    prop_i = PARENT_WEIGHT * par_i + NOISE_WEIGHT * spectrum_weight * noise_i
    rate1_r, rate1_i = tendency(prop_r, prop_i)
    mid_r = prop_r + TIME_STEP * rate1_r
    mid_i = prop_i + TIME_STEP * rate1_i
    rate2_r, rate2_i = tendency(mid_r, mid_i)
    fin_r = prop_r + 0.5 * TIME_STEP * (rate1_r + rate2_r)
    fin_i = prop_i + 0.5 * TIME_STEP * (rate1_i + rate2_i)
    out = fold(inverse(fin_r[None], fin_i[None]))
    return jnp.transpose(out, (1, 2, 0))


def solution(mesh):
    placed = (P("particle", "field", None), P(), P("particle", "field", None))
    return jax.shard_map(
        local, mesh=mesh, in_specs=placed, out_specs=P("particle", "field", None), check_vma=False
    )
```

```python
import math

import jax
import jax.numpy as jnp
from jax import lax
from jax.sharding import PartitionSpec as P

PARENT_WEIGHT = 0.8
NOISE_WEIGHT = 0.6
VISCOSITY = 0.05
TIME_STEP = 0.1
HIGHEST = lax.Precision.HIGH


def turn_phase(turns, length):
    reduced = turns % length
    reduced = jnp.where(reduced >= length // 2, reduced - length, reduced)
    angle = (2.0 * math.pi / length) * reduced.astype(jnp.float32)
    return jnp.cos(angle), jnp.sin(angle)


def split_cos(coarse, fine):
    return coarse[0] * fine[0] - coarse[1] * fine[1]


def split_sin(coarse, fine):
    return coarse[1] * fine[0] + coarse[0] * fine[1]


def slot_modes(length, parts):
    half = length // (2 * parts)
    order = lax.optimization_barrier(jnp.arange(length, dtype=jnp.int32))
    dest = order // (2 * half)
    t = order % (2 * half)
    mode = half * dest + t % half
    nyquist = order == half
    mode = jnp.where(nyquist, length // 2, mode)
    use_cos = (t < half) | nyquist
    return mode, use_cos


def grid_split(length):
    fine = 1 << ((length.bit_length() - 1) // 2)
    return fine, length // fine


def row_tables(length, parts):
    mode, use_cos = slot_modes(length, parts)
    fine, coarse = grid_split(length)
    hi = lax.optimization_barrier(jnp.arange(coarse, dtype=jnp.int32)) * fine
    lo = lax.optimization_barrier(jnp.arange(fine, dtype=jnp.int32))
    shift = jnp.where(use_cos, 0, length // 4)
    big = turn_phase(hi[:, None] * mode[None, :], length)
    small = turn_phase(lo[:, None] * mode[None, :] + shift[None, :], length)
    forward = split_cos(
        (big[0][:, None, :], big[1][:, None, :]), (small[0][None], small[1][None])
    ).reshape(length, length)
    weight = jnp.where((mode == 0) | (mode == length // 2), 1.0, 2.0) / float(length * length)
    big = turn_phase(mode[:, None] * hi[None, :], length)
    small = turn_phase(mode[:, None] * lo[None, :] + shift[:, None], length)
    inverse = split_cos(
        (big[0][:, :, None], big[1][:, :, None]), (small[0][:, None, :], small[1][:, None, :])
    ).reshape(length, length)
    return lax.optimization_barrier((inverse, weight[None, :] * forward))


def column_tables(length):
    fine, coarse = grid_split(length)
    hi = lax.optimization_barrier(jnp.arange(coarse, dtype=jnp.int32)) * fine
    lo = lax.optimization_barrier(jnp.arange(fine, dtype=jnp.int32))
    r = lax.optimization_barrier(jnp.arange(length, dtype=jnp.int32))
    folded = r > length // 2
    rmode = jnp.where(folded, r - length // 2, r)
    shift = jnp.where(folded, -(length // 4), 0)
    big = turn_phase(rmode[:, None] * hi[None, :], length)
    small = turn_phase(rmode[:, None] * lo[None, :] + shift[:, None], length)
    forward = split_cos(
        (big[0][:, :, None], big[1][:, :, None]), (small[0][:, None, :], small[1][:, None, :])
    ).reshape(length, length)
    big = turn_phase(hi[:, None] * rmode[None, :], length)
    small = turn_phase(lo[:, None] * rmode[None, :] + shift[None, :], length)
    inverse = split_cos(
        (big[0][:, None, :], big[1][:, None, :]), (small[0][None], small[1][None])
    ).reshape(length, length)
    return lax.optimization_barrier((forward, inverse))


def wave_tables(modes, length):
    signed = jnp.where(modes >= length // 2, modes - length, modes)
    wavenumber = 2.0 * math.pi / length * signed.astype(jnp.float32)
    slope = jnp.where(modes == length // 2, jnp.zeros_like(wavenumber), wavenumber)
    retained = jnp.where(3 * jnp.abs(signed) < length, 1.0, 0.0).astype(jnp.float32)
    return (wavenumber, slope, retained)


def local(vorticity, ancestors, noise):
    particle_count, row_count, length = vorticity.shape
    parts = lax.axis_size("field")
    half = length // (2 * parts)
    me = lax.axis_index("field")
    first_particle = lax.axis_index("particle") * particle_count

    row_fwd, row_inv = row_tables(length, parts)
    col_fwd, col_inv = column_tables(length)
    mid = length // 2

    slot = jnp.arange(half + 1, dtype=jnp.int32)
    mode_x = jnp.where(slot < half, half * me + slot, length // 2)
    position_y = jnp.arange(length, dtype=jnp.int32)
    mode_y = jnp.where(position_y > length // 2, length + length // 2 - position_y, position_y)
    wave_x, slope_x, kept_x = wave_tables(mode_x, length)
    wave_y, slope_y, kept_y = wave_tables(mode_y, length)
    squared = wave_x[None, :] ** 2 + wave_y[:, None] ** 2
    inverse_sq = jnp.where(squared > 0, 1.0 / jnp.where(squared > 0, squared, 1.0), 0.0)
    dealias = kept_x[None, :] * kept_y[:, None]
    spectrum_weight = 1.0 / (1.0 + squared)
    slope_x = slope_x[None, :]
    slope_y = slope_y[:, None]
    on_first = me == 0
    pair_mask = jnp.where(on_first & (slot[:half] == 0), 0.0, 1.0)[None, :]
    nyquist_gate = jnp.where(on_first, 1.0, 0.0)

    def forward(field_t):
        rows = jnp.einsum("ox,xy->oy", row_fwd, field_t, precision=HIGHEST)
        rows = rows.reshape(parts, 2 * half, row_count)
        cols = lax.all_to_all(rows, "field", split_axis=0, concat_axis=0, tiled=True)
        cols = jnp.swapaxes(cols, 1, 2).reshape(length, 2 * half)
        prod = jnp.einsum("ry,yt->rt", col_fwd, cols, precision=HIGHEST)
        pc = prod[: mid + 1]
        ps = prod[mid + 1 :]
        ps_ext = jnp.pad(ps, ((1, 1), (0, 0)))
        real_a = pc[:, :half] + pair_mask * ps_ext[:, half:]
        imag_a = pair_mask * pc[:, half:] - ps_ext[:, :half]
        real_b = pc[1:mid, :half] - pair_mask * ps[:, half:]
        imag_b = pair_mask * pc[1:mid, half:] + ps[:, :half]
        ny_real = nyquist_gate * jnp.concatenate([pc[:, half : half + 1], pc[1:mid, half : half + 1]], axis=0)
        ny_imag = nyquist_gate * jnp.concatenate([-ps_ext[:, half : half + 1], ps[:, half : half + 1]], axis=0)
        real = jnp.concatenate([jnp.concatenate([real_a, real_b], axis=0), ny_real], axis=1)
        imag = jnp.concatenate([jnp.concatenate([imag_a, imag_b], axis=0), ny_imag], axis=1)
        return real, imag

    def inverse(real, imag):
        batch = real.shape[0]
        n_slot = half + 1

        def plus(w):
            return jnp.concatenate([w[:, :1], w[:, 1:mid] + w[:, mid + 1 :], w[:, mid : mid + 1]], axis=1)

        def minus(w):
            return w[:, 1:mid] - w[:, mid + 1 :]

        v_real = jnp.concatenate([plus(real), -minus(imag)], axis=1)
        v_imag = jnp.concatenate([plus(imag), minus(real)], axis=1)
        stacked = jnp.concatenate([v_real, v_imag], axis=2)
        stacked = jnp.swapaxes(stacked, 0, 1).reshape(length, batch * 2 * n_slot)
        prod = jnp.einsum("yr,rn->yn", col_inv, stacked, precision=HIGHEST)
        prod = prod.reshape(length, batch, 2 * n_slot)
        z_real = prod[:, :, :n_slot]
        z_imag = prod[:, :, n_slot:]
        first_imag = jnp.where(on_first, z_real[:, :, half : half + 1], z_imag[:, :, 0:1])
        send = jnp.concatenate([z_real[:, :, :half], first_imag, z_imag[:, :, 1:half]], axis=2)
        send = send.reshape(parts, row_count, batch, 2 * half)
        back = lax.all_to_all(send, "field", split_axis=0, concat_axis=0, tiled=True)
        back = jnp.transpose(back, (0, 3, 2, 1)).reshape(length, batch * row_count)
        out = jnp.einsum("xs,sn->xn", row_inv, back, precision=HIGHEST)
        return out.reshape(length, batch, row_count)

    def tendency(real, imag):
        pot_r = real * inverse_sq
        pot_i = imag * inverse_sq
        fr = jnp.stack(
            [
                -slope_y * pot_i,
                slope_x * pot_i,
                -slope_x * imag,
                -slope_y * imag,
            ],
            axis=0,
        )
        fi = jnp.stack(
            [
                slope_y * pot_r,
                -slope_x * pot_r,
                slope_x * real,
                slope_y * real,
            ],
            axis=0,
        )
        physical = inverse(fr, fi)
        advection = physical[:, 0] * physical[:, 2] + physical[:, 1] * physical[:, 3]
        ar, ai = forward(advection)
        return (
            -dealias * ar - VISCOSITY * squared * real,
            -dealias * ai - VISCOSITY * squared * imag,
        )

    noise_r, noise_i = forward(noise[0].astype(jnp.float32).T)
    shard_rows = lax.all_gather(vorticity, "particle", axis=0, tiled=True)
    wanted = lax.dynamic_slice_in_dim(ancestors, first_particle, particle_count)
    parents = jnp.take(shard_rows, wanted, axis=0).astype(jnp.float32)
    par_r, par_i = forward(parents[0].T)

    prop_r = PARENT_WEIGHT * par_r + NOISE_WEIGHT * spectrum_weight * noise_r
    prop_i = PARENT_WEIGHT * par_i + NOISE_WEIGHT * spectrum_weight * noise_i
    def stage(_, carry):
        eval_r, eval_i, sum_r, sum_i = carry
        rate_r, rate_i = tendency(eval_r, eval_i)
        return (
            prop_r + TIME_STEP * rate_r,
            prop_i + TIME_STEP * rate_i,
            sum_r + rate_r,
            sum_i + rate_i,
        )

    zeros = jnp.zeros_like(prop_r)
    _, _, rates_r, rates_i = lax.fori_loop(0, 2, stage, (prop_r, prop_i, zeros, zeros))
    fin_r = prop_r + 0.5 * TIME_STEP * rates_r
    fin_i = prop_i + 0.5 * TIME_STEP * rates_i
    out = inverse(fin_r[None], fin_i[None])
    return jnp.transpose(out, (1, 2, 0))


def solution(mesh):
    placed = (P("particle", "field", None), P(), P("particle", "field", None))
    return jax.shard_map(
        local, mesh=mesh, in_specs=placed, out_specs=P("particle", "field", None), check_vma=False
    )
```
